512 devices in a mesh: outer: 16 (over z), inner: 32 (over y, x, core).
Axes of the slice: x: 4, y: 4, z: 16, core: 2. Of those that a mesh axis runs over, the one named last changes fastest.
Arguments:
- field_slab: float32 [512, 128, 4096], P(None, 'inner', 'outer'), may hold values from -48 to 48, as said below
- start_block: float32 [512, 256], replicated, may hold values from -6 to 6
Outputs:
- factor: float32 [512, 256], replicated
- core_fibres: float32 [256, 128, 4096], P('inner', None, 'outer')
The draws below stay inside these ranges and needn't reach their ends.
Inputs may be any that keep to these rules, and one draw needn't show every extreme that they name: `field_slab`: real values.
All inputs are finite; a program needn't handle non-finite values.
Results may differ from the reference program's by a relative error of at most 0.00016.
Values sent between devices are 32-bit elements; how exact they have to be, the bound alone decides.
No kernel may reach another device: no remote copies, remote signals or barrier semaphores. Data moves between devices by JAX's collectives and lax.ppermute only.
A program may use at most 64 MiB of HBM per device.

```python
import math
import jax
import jax.numpy as jnp
from jax import lax

I1 = 512
R1 = 256
ITERS = 2
I2 = 128
I3 = 4096


def draw_field_slab(key, part):
    noise_key = jax.random.fold_in(key, 11)
    row_key = jax.random.fold_in(key, 12)
    col_key = jax.random.fold_in(key, 13)
    noise = jnp.clip(jax.random.normal(noise_key, (I1, I2, I3), jnp.float32), -4.0, 4.0)
    row_scale = jnp.exp(jax.random.uniform(row_key, (I1, 1, 1), jnp.float32, 0.0, math.log(4.0)))
    col_scale = jnp.exp(jax.random.uniform(col_key, (1, I2, I3), jnp.float32, 0.0, math.log(10.0)))
    second_pos = jnp.arange(I2, dtype=jnp.float32).reshape(1, I2, 1) / I2
    third_pos = jnp.arange(I3, dtype=jnp.float32).reshape(1, 1, I3) / I3
    ramp_scale = jnp.exp(0.55 * (second_pos + third_pos))
    return 0.1 * noise * row_scale * col_scale * ramp_scale


def normal_values(rng, shape, width, most, held_as=jnp.bfloat16):
    values = width * jax.random.normal(rng, shape, jnp.float32)
    return jnp.clip(values, min=-most, max=most).astype(held_as)


def setup_inputs(seed: int = 0) -> dict:
    key_list = jax.random.split(jax.random.key(seed), 3)
    return {
        "field_slab": draw_field_slab(jax.random.fold_in(key_list[2], 71), 0),
        "start_block": normal_values(key_list[1], (I1, R1), 1.0, 6.0, jnp.float32),
    }


def orthonormal(block):
    gram_small = jnp.dot(block.T.astype(jnp.float32), block.astype(jnp.float32), precision=lax.Precision.HIGHEST, preferred_element_type=jnp.float32)
    chol_factor = jnp.linalg.cholesky(gram_small)
    return lax.linalg.triangular_solve(chol_factor, block, left_side=False, lower=True, transpose_a=True)

def reference(field_slab, start_block):
    unfolded = field_slab.reshape(I1, I2 * I3)
    gram_total = jnp.dot(unfolded.astype(jnp.float32), unfolded.T.astype(jnp.float32), precision=lax.Precision.HIGHEST, preferred_element_type=jnp.float32)
    subspace = orthonormal(start_block)
    for sweep_index in range(ITERS):
        subspace = orthonormal(jnp.dot(gram_total.astype(jnp.float32), subspace.astype(jnp.float32), precision=lax.Precision.HIGHEST, preferred_element_type=jnp.float32))
    core_block = jnp.dot(subspace.T.astype(jnp.float32), unfolded.astype(jnp.float32), precision=lax.Precision.HIGHEST, preferred_element_type=jnp.float32)
    return (subspace, core_block.reshape(R1, I2, I3))
```

```python
import jax
import jax.numpy as jnp
from jax import lax
from jax.sharding import PartitionSpec as P

ITERS = 2


def product(first_mat, second_mat):
    return jnp.dot(
        first_mat, second_mat, precision=lax.Precision.HIGHEST, preferred_element_type=jnp.float32
    )


def orthonormal(block):
    chol_factor = jnp.linalg.cholesky(product(block.T, block))
    return lax.linalg.triangular_solve(
        chol_factor, block, left_side=False, lower=True, transpose_a=True
    )


def scatter_sum(block, axis_name, parts):
    pieces = block.reshape(parts, block.shape[0] // parts, *block.shape[1:])
    return lax.all_to_all(pieces, axis_name, 0, 0, tiled=True).sum(0)


def gather_rows(block, axis_name, parts):
    copies = jnp.broadcast_to(block[None], (parts,) + block.shape)
    gathered = lax.all_to_all(copies, axis_name, 0, 0, tiled=True)
    return gathered.reshape(parts * block.shape[0], *block.shape[1:])


def sum_everywhere(block, sizes):
    partial = scatter_sum(block, "inner", sizes["inner"])
    partial = scatter_sum(partial, "outer", sizes["outer"])
    partial = gather_rows(partial, "outer", sizes["outer"])
    return gather_rows(partial, "inner", sizes["inner"])


def on_device(field_slab, start_block, sizes):
    order_rows = field_slab.shape[0]
    local_shape = field_slab.shape
    unfolded = field_slab.reshape(order_rows, local_shape[1] * local_shape[2])
    gram_local = product(unfolded, unfolded.T)
    subspace = orthonormal(start_block)
    gram_total = sum_everywhere(gram_local, sizes)
    for sweep_index in range(ITERS):
        subspace = orthonormal(product(gram_total, subspace))
    core_block = product(subspace.T, unfolded).reshape(
        subspace.shape[1], local_shape[1], local_shape[2]
    )
    core_fibres = lax.all_to_all(core_block, "inner", split_axis=0, concat_axis=1, tiled=True)
    return (subspace, core_fibres)


def solution(mesh):
    sizes = dict(mesh.shape)
    in_specs = (P(None, "inner", "outer"), P())
    out_specs = (P(), P("inner", None, "outer"))
    return jax.shard_map(
        lambda f, s: on_device(f, s, sizes),
        mesh=mesh, in_specs=in_specs, out_specs=out_specs, check_vma=False,
    )
```

```python
import jax
import jax.numpy as jnp
from jax import lax
from jax.experimental import pallas as pl
from jax.experimental.pallas import tpu as pltpu
from jax.sharding import PartitionSpec as P

ITERS = 2

PANEL = 64
UNROLL = 8


def product(first_mat, second_mat):
    return jnp.dot(
        first_mat, second_mat, precision=lax.Precision.HIGHEST, preferred_element_type=jnp.float32
    )


def mat(first, second):
    return jnp.dot(first, second, precision=lax.Precision.HIGHEST, preferred_element_type=jnp.float32)


def mat_nt(first, second):
    return lax.dot_general(
        first, second, (((1,), (1,)), ((), ())),
        precision=lax.Precision.HIGHEST, preferred_element_type=jnp.float32,
    )


def leaf_inverse_factor(diag_block):
    size = diag_block.shape[0]
    sub = lax.broadcasted_iota(jnp.int32, (size, size), 0)
    lane = lax.broadcasted_iota(jnp.int32, (size, size), 1)
    sub_col = lax.broadcasted_iota(jnp.int32, (size, 1), 0)
    lane_row = lax.broadcasted_iota(jnp.int32, (1, size), 1)

    def step(j, carry):
        rest, inv_rows = carry
        row = jnp.sum(jnp.where(sub == j, rest, 0.0), axis=0, keepdims=True)
        col = jnp.sum(jnp.where(lane == j, rest, 0.0), axis=1, keepdims=True)
        pivot = jnp.sum(jnp.where(lane_row == j, row, 0.0), axis=1, keepdims=True)
        scale = 1.0 / jnp.sqrt(pivot)
        factor_col = jnp.where(sub_col >= j, col * scale, 0.0)
        factor_row = jnp.where(lane_row >= j, row * scale, 0.0)
        rest = rest - factor_col * factor_row
        solved = jnp.sum(jnp.where(sub == j, inv_rows, 0.0), axis=0, keepdims=True) * scale
        below = jnp.where(sub_col > j, factor_col, 0.0)
        inv_rows = jnp.where(sub == j, solved, inv_rows - below * solved)
        return rest, inv_rows

    start = jnp.where(sub == lane, 1.0, 0.0).astype(jnp.float32)
    _, inv_rows = lax.fori_loop(0, size, step, (diag_block, start), unroll=UNROLL)
    return inv_rows


def orth_kernel(gram_ref, block_ref, out_ref, rest_ref, inv_ref):
    order = gram_ref.shape[0]
    rest_ref[...] = gram_ref[...]
    eye_sub = lax.broadcasted_iota(jnp.int32, (order, order), 0)
    eye_lane = lax.broadcasted_iota(jnp.int32, (order, order), 1)
    inv_ref[...] = jnp.where(eye_sub == eye_lane, 1.0, 0.0).astype(jnp.float32)
    rows = lax.broadcasted_iota(jnp.int32, (order, 1), 0)
    for panel in range(order // PANEL):
        low = panel * PANEL
        pick_sub = lax.broadcasted_iota(jnp.int32, (PANEL, order), 0)
        pick_lane = lax.broadcasted_iota(jnp.int32, (PANEL, order), 1)
        pick = jnp.where(pick_lane == pick_sub + low, 1.0, 0.0).astype(jnp.float32)
        cols = mat_nt(rest_ref[...], pick)
        diag_inv = leaf_inverse_factor(cols[low:low + PANEL, :])
        factor = jnp.where(rows >= low, mat_nt(cols, diag_inv), 0.0)
        rest_ref[...] = rest_ref[...] - mat_nt(factor, factor)
        solved = mat(diag_inv, inv_ref[low:low + PANEL, :])
        below = jnp.where(rows >= low + PANEL, factor, 0.0)
        inv_ref[...] = inv_ref[...] - mat(below, solved)
        inv_ref[low:low + PANEL, :] = solved
    out_ref[...] = mat_nt(block_ref[...], inv_ref[...])


def orthonormal(block):
    gram = jnp.dot(block.T, block, precision=lax.Precision.HIGHEST, preferred_element_type=jnp.float32)
    order = block.shape[1]
    return pl.pallas_call(
        orth_kernel,
        out_shape=jax.ShapeDtypeStruct(block.shape, jnp.float32),
        scratch_shapes=[pltpu.VMEM((order, order), jnp.float32), pltpu.VMEM((order, order), jnp.float32)],
    )(gram, block)


def scatter_sum(block, axis_name, parts):
    pieces = block.reshape(parts, block.shape[0] // parts, *block.shape[1:])
    return lax.all_to_all(pieces, axis_name, 0, 0, tiled=True).sum(0)


def gather_rows(block, axis_name, parts):
    copies = jnp.broadcast_to(block[None], (parts,) + block.shape)
    gathered = lax.all_to_all(copies, axis_name, 0, 0, tiled=True)
    return gathered.reshape(parts * block.shape[0], *block.shape[1:])


def sum_everywhere(block, sizes):
    partial = scatter_sum(block, "inner", sizes["inner"])
    partial = scatter_sum(partial, "outer", sizes["outer"])
    partial = gather_rows(partial, "outer", sizes["outer"])
    return gather_rows(partial, "inner", sizes["inner"])


def on_device(field_slab, start_block, sizes):
    order_rows = field_slab.shape[0]
    local_shape = field_slab.shape
    unfolded = field_slab.reshape(order_rows, local_shape[1] * local_shape[2])
    gram_local = product(unfolded, unfolded.T)
    subspace = orthonormal(start_block)
    gram_total = sum_everywhere(gram_local, sizes)
    for sweep_index in range(ITERS):
        subspace = orthonormal(product(gram_total, subspace))
    core_block = product(subspace.T, unfolded).reshape(
        subspace.shape[1], local_shape[1], local_shape[2]
    )
    core_fibres = lax.all_to_all(core_block, "inner", split_axis=0, concat_axis=1, tiled=True)
    return (subspace, core_fibres)


def solution(mesh):
    sizes = dict(mesh.shape)
    in_specs = (P(None, "inner", "outer"), P())
    out_specs = (P(), P("inner", None, "outer"))
    return jax.shard_map(
        lambda f, s: on_device(f, s, sizes),
        mesh=mesh, in_specs=in_specs, out_specs=out_specs, check_vma=False,
    )
```

```python
import jax
import jax.numpy as jnp
from jax import lax
from jax.experimental import pallas as pl
from jax.experimental.pallas import tpu as pltpu
from jax.sharding import PartitionSpec as P

ITERS = 2

PANEL = 64
UNROLL = 8


def product(first_mat, second_mat):
    return jnp.dot(
        first_mat, second_mat, precision=lax.Precision.HIGHEST, preferred_element_type=jnp.float32
    )


def mat(first, second):
    return jnp.dot(first, second, precision=lax.Precision.HIGHEST, preferred_element_type=jnp.float32)


def mat_nt(first, second):
    return lax.dot_general(
        first, second, (((1,), (1,)), ((), ())),
        precision=lax.Precision.HIGHEST, preferred_element_type=jnp.float32,
    )


def leaf_inverse_factor(diag_block):
    size = diag_block.shape[0]
    sub = lax.broadcasted_iota(jnp.int32, (size, size), 0)
    lane = lax.broadcasted_iota(jnp.int32, (size, size), 1)
    sub_col = lax.broadcasted_iota(jnp.int32, (size, 1), 0)
    lane_row = lax.broadcasted_iota(jnp.int32, (1, size), 1)

    def step(j, carry):
        rest, inv_rows = carry
        row = jnp.sum(jnp.where(sub == j, rest, 0.0), axis=0, keepdims=True)
        col = jnp.sum(jnp.where(lane == j, rest, 0.0), axis=1, keepdims=True)
        pivot = jnp.sum(jnp.where(lane_row == j, row, 0.0), axis=1, keepdims=True)
        scale = lax.rsqrt(pivot)
        factor_col = jnp.where(sub_col >= j, col * scale, 0.0)
        factor_row = jnp.where(lane_row >= j, row * scale, 0.0)
        rest = rest - factor_col * factor_row
        solved = jnp.sum(jnp.where(sub == j, inv_rows, 0.0), axis=0, keepdims=True) * scale
        below = jnp.where(sub_col > j, factor_col, 0.0)
        inv_rows = jnp.where(sub == j, solved, inv_rows - below * solved)
        return rest, inv_rows

    start = jnp.where(sub == lane, 1.0, 0.0).astype(jnp.float32)
    _, inv_rows = lax.fori_loop(0, size, step, (diag_block, start), unroll=UNROLL)
    return inv_rows


def orth_kernel(gram_ref, block_ref, out_ref, rest_ref, inv_ref):
    order = gram_ref.shape[0]
    rest_ref[...] = gram_ref[...]
    eye_sub = lax.broadcasted_iota(jnp.int32, (order, order), 0)
    eye_lane = lax.broadcasted_iota(jnp.int32, (order, order), 1)
    inv_ref[...] = jnp.where(eye_sub == eye_lane, 1.0, 0.0).astype(jnp.float32)
    rows = lax.broadcasted_iota(jnp.int32, (order, 1), 0)
    for panel in range(order // PANEL):
        low = panel * PANEL
        pick_sub = lax.broadcasted_iota(jnp.int32, (PANEL, order), 0)
        pick_lane = lax.broadcasted_iota(jnp.int32, (PANEL, order), 1)
        pick = jnp.where(pick_lane == pick_sub + low, 1.0, 0.0).astype(jnp.float32)
        cols = mat_nt(rest_ref[...], pick)
        diag_inv = leaf_inverse_factor(cols[low:low + PANEL, :])
        factor = jnp.where(rows >= low, mat_nt(cols, diag_inv), 0.0)
        rest_ref[...] = rest_ref[...] - mat_nt(factor, factor)
        solved = mat(diag_inv, inv_ref[low:low + PANEL, :])
        below = jnp.where(rows >= low + PANEL, factor, 0.0)
        inv_ref[...] = inv_ref[...] - mat(below, solved)
        inv_ref[low:low + PANEL, :] = solved
    out_ref[...] = mat_nt(block_ref[...], inv_ref[...])


def orthonormal(block):
    gram = jnp.dot(block.T, block, precision=lax.Precision.HIGHEST, preferred_element_type=jnp.float32)
    order = block.shape[1]
    return pl.pallas_call(
        orth_kernel,
        out_shape=jax.ShapeDtypeStruct(block.shape, jnp.float32),
        scratch_shapes=[pltpu.VMEM((order, order), jnp.float32), pltpu.VMEM((order, order), jnp.float32)],
    )(gram, block)


def scatter_sum(block, axis_name, parts):
    pieces = block.reshape(parts, block.shape[0] // parts, *block.shape[1:])
    return lax.all_to_all(pieces, axis_name, 0, 0, tiled=True).sum(0)


def gather_rows(block, axis_name, parts):
    copies = jnp.broadcast_to(block[None], (parts,) + block.shape)
    gathered = lax.all_to_all(copies, axis_name, 0, 0, tiled=True)
    return gathered.reshape(parts * block.shape[0], *block.shape[1:])


def sum_everywhere(block, sizes):
    partial = scatter_sum(block, "inner", sizes["inner"])
    partial = scatter_sum(partial, "outer", sizes["outer"])
    partial = gather_rows(partial, "outer", sizes["outer"])
    return gather_rows(partial, "inner", sizes["inner"])


def on_device(field_slab, start_block, sizes):
    gram_local = lax.dot_general(
        field_slab, field_slab, (((1, 2), (1, 2)), ((), ())),
        precision=lax.Precision.HIGHEST, preferred_element_type=jnp.float32,
    )
    subspace = orthonormal(start_block)
    gram_total = sum_everywhere(gram_local, sizes)
    for sweep_index in range(ITERS):
        subspace = orthonormal(product(gram_total, subspace))
    core_block = lax.dot_general(
        subspace, field_slab, (((0,), (0,)), ((), ())),
        precision=lax.Precision.HIGHEST, preferred_element_type=jnp.float32,
    )
    core_fibres = lax.all_to_all(core_block, "inner", split_axis=0, concat_axis=1, tiled=True)
    return (subspace, core_fibres)


def solution(mesh):
    sizes = dict(mesh.shape)
    in_specs = (P(None, "inner", "outer"), P())
    out_specs = (P(), P("inner", None, "outer"))
    return jax.shard_map(
        lambda f, s: on_device(f, s, sizes),
        mesh=mesh, in_specs=in_specs, out_specs=out_specs, check_vma=False,
    )
```

```python
import jax
import jax.numpy as jnp
from jax import lax
from jax.experimental import pallas as pl
from jax.experimental.pallas import tpu as pltpu
from jax.sharding import PartitionSpec as P

ITERS = 2

PANEL = 64
UNROLL = 1


def product(first_mat, second_mat):
    return jnp.dot(
        first_mat, second_mat, precision=lax.Precision.HIGHEST, preferred_element_type=jnp.float32
    )


def mat(first, second):
    return jnp.dot(first, second, precision=lax.Precision.HIGHEST, preferred_element_type=jnp.float32)


def mat_nt(first, second):
    return lax.dot_general(
        first, second, (((1,), (1,)), ((), ())),
        precision=lax.Precision.HIGHEST, preferred_element_type=jnp.float32,
    )


GROUP = 8


def leaf_inverse_factor(diag_block):
    size = diag_block.shape[0]
    wide = 2 * size
    sub = lax.broadcasted_iota(jnp.int32, (size, wide), 0)
    lane = lax.broadcasted_iota(jnp.int32, (size, wide), 1)
    sub_col = lax.broadcasted_iota(jnp.int32, (size, 1), 0)
    lane_row = lax.broadcasted_iota(jnp.int32, (1, wide), 1)
    joined = diag_block + jnp.where(lane == sub + size, 1.0, 0.0).astype(jnp.float32)

    def step(group, carry):
        rest, solved_rows = carry
        first = group * GROUP
        rows = [jnp.sum(jnp.where(sub == first + i, rest, 0.0), axis=0, keepdims=True) for i in range(GROUP)]
        cols = [jnp.sum(jnp.where(lane == first + i, rest, 0.0), axis=1, keepdims=True) for i in range(GROUP)]
        pivots = [
            [jnp.sum(jnp.where(lane_row == first + m, rows[i], 0.0), axis=1, keepdims=True) for m in range(i + 1)]
            for i in range(GROUP)
        ]
        low = [[None] * GROUP for _ in range(GROUP)]
        scales = []
        for i in range(GROUP):
            for r in range(i, GROUP):
                value = pivots[r][i]
                for m in range(i):
                    value = value - low[r][m] * low[i][m]
                if r == i:
                    scale = lax.rsqrt(value)
                    scales.append(scale)
                    low[i][i] = value * scale
                else:
                    low[r][i] = value * scales[i]
        factor_rows, factor_cols = [], []
        for i in range(GROUP):
            row, col = rows[i], cols[i]
            for m in range(i):
                row = row - low[i][m] * factor_rows[m]
                col = col - low[i][m] * factor_cols[m]
            factor_rows.append(jnp.where(lane_row >= first + i, row * scales[i], 0.0))
            factor_cols.append(jnp.where(sub_col >= first + i, col * scales[i], 0.0))
        for i in range(GROUP):
            rest = rest - factor_cols[i] * factor_rows[i]
            solved_rows = jnp.where(sub == first + i, factor_rows[i], solved_rows)
        return rest, solved_rows

    _, solved_rows = lax.fori_loop(0, size // GROUP, step, (joined, jnp.zeros_like(joined)), unroll=UNROLL)
    swapped = pltpu.roll(solved_rows, size, 1)
    return jnp.where(lane < size, swapped, 0.0)


def orth_kernel(gram_ref, block_ref, out_ref, rest_ref, inv_ref):
    order = gram_ref.shape[0]
    wide = 2 * PANEL
    rest_ref[...] = gram_ref[...]
    eye_sub = lax.broadcasted_iota(jnp.int32, inv_ref.shape, 0)
    eye_lane = lax.broadcasted_iota(jnp.int32, inv_ref.shape, 1)
    inv_ref[...] = jnp.where(eye_sub == eye_lane, 1.0, 0.0).astype(jnp.float32)
    rows = lax.broadcasted_iota(jnp.int32, (order, 1), 0)
    pick_sub = lax.broadcasted_iota(jnp.int32, (wide, order), 0)
    pick_lane = lax.broadcasted_iota(jnp.int32, (wide, order), 1)
    for panel in range(order // PANEL):
        low = panel * PANEL
        pick = jnp.where((pick_lane == pick_sub + low) & (pick_sub < PANEL), 1.0, 0.0)
        cols = mat_nt(rest_ref[...], pick.astype(jnp.float32))
        diag_inv = leaf_inverse_factor(cols[low:low + PANEL, :])
        factor = jnp.where(rows >= low, mat_nt(cols, diag_inv), 0.0)
        rest_ref[...] = rest_ref[...] - mat_nt(factor, factor)
        solved = mat(diag_inv, inv_ref[low:low + wide, :])
        below = jnp.where(rows >= low + PANEL, factor, 0.0)
        inv_ref[0:order, :] = inv_ref[0:order, :] - mat(below, solved)
        inv_ref[low:low + PANEL, :] = solved
    out_ref[...] = mat_nt(block_ref[...], inv_ref[0:order, :])


def orthonormal(block):
    gram = jnp.dot(block.T, block, precision=lax.Precision.HIGHEST, preferred_element_type=jnp.float32)
    order = block.shape[1]
    return pl.pallas_call(
        orth_kernel,
        out_shape=jax.ShapeDtypeStruct(block.shape, jnp.float32),
        scratch_shapes=[pltpu.VMEM((order, order), jnp.float32), pltpu.VMEM((order + PANEL, order), jnp.float32)],
    )(gram, block)


def scatter_sum(block, axis_name, parts):
    pieces = block.reshape(parts, block.shape[0] // parts, *block.shape[1:])
    return lax.all_to_all(pieces, axis_name, 0, 0, tiled=True).sum(0)


def gather_rows(block, axis_name, parts):
    copies = jnp.broadcast_to(block[None], (parts,) + block.shape)
    gathered = lax.all_to_all(copies, axis_name, 0, 0, tiled=True)
    return gathered.reshape(parts * block.shape[0], *block.shape[1:])


def sum_everywhere(block, sizes):
    partial = scatter_sum(block, "inner", sizes["inner"])
    partial = scatter_sum(partial, "outer", sizes["outer"])
    partial = gather_rows(partial, "outer", sizes["outer"])
    return gather_rows(partial, "inner", sizes["inner"])


def on_device(field_slab, start_block, sizes):
    gram_local = lax.dot_general(
        field_slab, field_slab, (((1, 2), (1, 2)), ((), ())),
        precision=lax.Precision.HIGHEST, preferred_element_type=jnp.float32,
    )
    subspace = orthonormal(start_block)
    gram_total = sum_everywhere(gram_local, sizes)
    for sweep_index in range(ITERS):
        subspace = orthonormal(product(gram_total, subspace))
    core_block = lax.dot_general(
        subspace, field_slab, (((0,), (0,)), ((), ())),
        precision=lax.Precision.HIGHEST, preferred_element_type=jnp.float32,
    )
    core_fibres = lax.all_to_all(core_block, "inner", split_axis=0, concat_axis=1, tiled=True)
    return (subspace, core_fibres)


def solution(mesh):
    sizes = dict(mesh.shape)
    in_specs = (P(None, "inner", "outer"), P())
    out_specs = (P(), P("inner", None, "outer"))
    return jax.shard_map(
        lambda f, s: on_device(f, s, sizes),
        mesh=mesh, in_specs=in_specs, out_specs=out_specs, check_vma=False,
    )
```

```python
import jax
import jax.numpy as jnp
from jax import lax
from jax.experimental import pallas as pl
from jax.experimental.pallas import tpu as pltpu
from jax.sharding import PartitionSpec as P

ITERS = 2

PANEL = 64
UNROLL = 1


def product(first_mat, second_mat):
    return jnp.dot(
        first_mat, second_mat, precision=lax.Precision.HIGHEST, preferred_element_type=jnp.float32
    )


def mat(first, second):
    return jnp.dot(first, second, precision=lax.Precision.HIGHEST, preferred_element_type=jnp.float32)


def mat_nt(first, second):
    return lax.dot_general(
        first, second, (((1,), (1,)), ((), ())),
        precision=lax.Precision.HIGHEST, preferred_element_type=jnp.float32,
    )


GROUP = 8


def leaf_inverse_factor(diag_block):
    size = diag_block.shape[0]
    wide = 2 * size
    sub = lax.broadcasted_iota(jnp.int32, (size, wide), 0)
    lane = lax.broadcasted_iota(jnp.int32, (size, wide), 1)
    sub_col = lax.broadcasted_iota(jnp.int32, (size, 1), 0)
    lane_row = lax.broadcasted_iota(jnp.int32, (1, wide), 1)
    joined = diag_block + jnp.where(lane == sub + size, 1.0, 0.0).astype(jnp.float32)

    def step(group, carry):
        rest, solved_rows = carry
        first = group * GROUP
        rows = [jnp.sum(jnp.where(sub == first + i, rest, 0.0), axis=0, keepdims=True) for i in range(GROUP)]
        cols = [jnp.sum(jnp.where(lane == first + i, rest, 0.0), axis=1, keepdims=True) for i in range(GROUP)]
        pivots = [
            [jnp.sum(jnp.where(lane_row == first + m, rows[i], 0.0), axis=1, keepdims=True) for m in range(i + 1)]
            for i in range(GROUP)
        ]
        low = [[None] * GROUP for _ in range(GROUP)]
        scales = []
        for i in range(GROUP):
            for r in range(i, GROUP):
                value = pivots[r][i]
                for m in range(i):
                    value = value - low[r][m] * low[i][m]
                if r == i:
                    scale = lax.rsqrt(value)
                    scales.append(scale)
                    low[i][i] = value * scale
                else:
                    low[r][i] = value * scales[i]
        factor_rows, factor_cols = [], []
        for i in range(GROUP):
            row, col = rows[i], cols[i]
            for m in range(i):
                row = row - low[i][m] * factor_rows[m]
                col = col - low[i][m] * factor_cols[m]
            factor_rows.append(jnp.where(lane_row >= first + i, row * scales[i], 0.0))
            factor_cols.append(jnp.where(sub_col >= first + i, col * scales[i], 0.0))
        for i in range(GROUP):
            rest = rest - factor_cols[i] * factor_rows[i]
            solved_rows = jnp.where(sub == first + i, factor_rows[i], solved_rows)
        return rest, solved_rows

    _, solved_rows = lax.fori_loop(0, size // GROUP, step, (joined, jnp.zeros_like(joined)), unroll=UNROLL)
    swapped = pltpu.roll(solved_rows, size, 1)
    return jnp.where(lane < size, swapped, 0.0)


def orth_kernel(gram_ref, block_ref, out_ref, rest_ref, inv_ref):
    order = gram_ref.shape[0]
    wide = 2 * PANEL
    rest_ref[...] = gram_ref[...]
    eye_sub = lax.broadcasted_iota(jnp.int32, inv_ref.shape, 0)
    eye_lane = lax.broadcasted_iota(jnp.int32, inv_ref.shape, 1)
    inv_ref[...] = jnp.where(eye_sub == eye_lane, 1.0, 0.0).astype(jnp.float32)
    rows = lax.broadcasted_iota(jnp.int32, (order, 1), 0)
    lanes = lax.broadcasted_iota(jnp.int32, (order, wide), 1)
    panels = order // PANEL
    for panel in range(panels):
        low = panel * PANEL
        base = low - low % wide
        cols = rest_ref[:, base:base + wide]
        if low % wide:
            cols = pltpu.roll(cols, wide - low % wide, 1)
        cols = jnp.where(lanes < PANEL, cols, 0.0)
        diag_inv = leaf_inverse_factor(cols[low:low + PANEL, :])
        factor = jnp.where(rows >= low, mat_nt(cols, diag_inv), 0.0)
        solved = mat(diag_inv, inv_ref[low:low + wide, :])
        if panel + 1 < panels:
            rest_ref[...] = rest_ref[...] - mat_nt(factor, factor)
            below = jnp.where(rows >= low + PANEL, factor, 0.0)
            inv_ref[0:order, :] = inv_ref[0:order, :] - mat(below, solved)
        inv_ref[low:low + PANEL, :] = solved
    out_ref[...] = mat_nt(block_ref[...], inv_ref[0:order, :])


def orthonormal(block):
    gram = jnp.dot(block.T, block, precision=lax.Precision.HIGHEST, preferred_element_type=jnp.float32)
    order = block.shape[1]
    return pl.pallas_call(
        orth_kernel,
        out_shape=jax.ShapeDtypeStruct(block.shape, jnp.float32),
        scratch_shapes=[pltpu.VMEM((order, order), jnp.float32), pltpu.VMEM((order + PANEL, order), jnp.float32)],
    )(gram, block)


def scatter_sum(block, axis_name, parts):
    pieces = block.reshape(parts, block.shape[0] // parts, *block.shape[1:])
    return lax.all_to_all(pieces, axis_name, 0, 0, tiled=True).sum(0)


def gather_rows(block, axis_name, parts):
    copies = jnp.broadcast_to(block[None], (parts,) + block.shape)
    gathered = lax.all_to_all(copies, axis_name, 0, 0, tiled=True)
    return gathered.reshape(parts * block.shape[0], *block.shape[1:])


def sum_everywhere(block, sizes):
    partial = scatter_sum(block, "inner", sizes["inner"])
    partial = scatter_sum(partial, "outer", sizes["outer"])
    partial = gather_rows(partial, "outer", sizes["outer"])
    return gather_rows(partial, "inner", sizes["inner"])


def on_device(field_slab, start_block, sizes):
    gram_local = lax.dot_general(
        field_slab, field_slab, (((1, 2), (1, 2)), ((), ())),
        precision=lax.Precision.HIGHEST, preferred_element_type=jnp.float32,
    )
    subspace = orthonormal(start_block)
    gram_total = sum_everywhere(gram_local, sizes)
    for sweep_index in range(ITERS):
        subspace = orthonormal(product(gram_total, subspace))
    core_block = lax.dot_general(
        subspace, field_slab, (((0,), (0,)), ((), ())),
        precision=lax.Precision.HIGHEST, preferred_element_type=jnp.float32,
    )
    core_fibres = lax.all_to_all(core_block, "inner", split_axis=0, concat_axis=1, tiled=True)
    return (subspace, core_fibres)


def solution(mesh):
    sizes = dict(mesh.shape)
    in_specs = (P(None, "inner", "outer"), P())
    out_specs = (P(), P("inner", None, "outer"))
    return jax.shard_map(
        lambda f, s: on_device(f, s, sizes),
        mesh=mesh, in_specs=in_specs, out_specs=out_specs, check_vma=False,
    )
```

```python
import jax
import jax.numpy as jnp
from jax import lax
from jax.experimental import pallas as pl
from jax.experimental.pallas import tpu as pltpu
from jax.sharding import PartitionSpec as P

ITERS = 2

PANEL = 64
UNROLL = 1


def product(first_mat, second_mat):
    return jnp.dot(
        first_mat, second_mat, precision=lax.Precision.HIGHEST, preferred_element_type=jnp.float32
    )


def mat(first, second):
    return jnp.dot(first, second, precision=lax.Precision.HIGHEST, preferred_element_type=jnp.float32)


def mat_nt(first, second):
    return lax.dot_general(
        first, second, (((1,), (1,)), ((), ())),
        precision=lax.Precision.HIGHEST, preferred_element_type=jnp.float32,
    )


GROUP = 8


def leaf_inverse_factor(diag_block):
    size = diag_block.shape[0]
    wide = 2 * size
    sub = lax.broadcasted_iota(jnp.int32, (size, wide), 0)
    lane = lax.broadcasted_iota(jnp.int32, (size, wide), 1)
    sub_col = lax.broadcasted_iota(jnp.int32, (size, 1), 0)
    lane_row = lax.broadcasted_iota(jnp.int32, (1, wide), 1)
    joined = diag_block + jnp.where(lane == sub + size, 1.0, 0.0).astype(jnp.float32)

    def step(group, carry):
        rest, solved_rows = carry
        first = group * GROUP
        rows = [jnp.sum(jnp.where(sub == first + i, rest, 0.0), axis=0, keepdims=True) for i in range(GROUP)]
        cols = [jnp.sum(jnp.where(lane == first + i, rest, 0.0), axis=1, keepdims=True) for i in range(GROUP)]
        pivots = [
            [jnp.sum(jnp.where(lane_row == first + m, rows[i], 0.0), axis=1, keepdims=True) for m in range(i + 1)]
            for i in range(GROUP)
        ]
        low = [[None] * GROUP for _ in range(GROUP)]
        scales = []
        for i in range(GROUP):
            for r in range(i, GROUP):
                value = pivots[r][i]
                for m in range(i):
                    value = value - low[r][m] * low[i][m]
                if r == i:
                    scale = lax.rsqrt(value)
                    scales.append(scale)
                    low[i][i] = value * scale
                else:
                    low[r][i] = value * scales[i]
        factor_rows, factor_cols = [], []
        for i in range(GROUP):
            row, col = rows[i], cols[i]
            for m in range(i):
                row = row - low[i][m] * factor_rows[m]
                col = col - low[i][m] * factor_cols[m]
            factor_rows.append(jnp.where(lane_row >= first + i, row * scales[i], 0.0))
            factor_cols.append(jnp.where(sub_col >= first + i, col * scales[i], 0.0))
        for i in range(GROUP):
            rest = rest - factor_cols[i] * factor_rows[i]
            solved_rows = jnp.where(sub == first + i, factor_rows[i], solved_rows)
        return rest, solved_rows

    _, solved_rows = lax.fori_loop(0, size // GROUP, step, (joined, jnp.zeros_like(joined)), unroll=UNROLL)
    swapped = pltpu.roll(solved_rows, size, 1)
    return jnp.where(lane < size, swapped, 0.0)


def mat_tn(first, second):
    return lax.dot_general(
        first, second, (((0,), (0,)), ((), ())),
        precision=lax.Precision.HIGHEST, preferred_element_type=jnp.float32,
    )


def factor_and_apply(block_ref, out_ref, rest_ref, inv_ref):
    order = block_ref.shape[1]
    wide = 2 * PANEL
    block = block_ref[...]
    rest_ref[...] = mat_tn(block, block)
    eye_sub = lax.broadcasted_iota(jnp.int32, inv_ref.shape, 0)
    eye_lane = lax.broadcasted_iota(jnp.int32, inv_ref.shape, 1)
    inv_ref[...] = jnp.where(eye_sub == eye_lane, 1.0, 0.0).astype(jnp.float32)
    rows = lax.broadcasted_iota(jnp.int32, (order, 1), 0)
    lanes = lax.broadcasted_iota(jnp.int32, (order, wide), 1)
    panels = order // PANEL
    for panel in range(panels):
        low = panel * PANEL
        base = low - low % wide
        cols = rest_ref[:, base:base + wide]
        if low % wide:
            cols = pltpu.roll(cols, wide - low % wide, 1)
        cols = jnp.where(lanes < PANEL, cols, 0.0)
        diag_inv = leaf_inverse_factor(cols[low:low + PANEL, :])
        factor = jnp.where(rows >= low, mat_nt(cols, diag_inv), 0.0)
        solved = mat(diag_inv, inv_ref[low:low + wide, :])
        if panel + 1 < panels:
            rest_ref[...] = rest_ref[...] - mat_nt(factor, factor)
            below = jnp.where(rows >= low + PANEL, factor, 0.0)
            inv_ref[0:order, :] = inv_ref[0:order, :] - mat(below, solved)
        inv_ref[low:low + PANEL, :] = solved
    out_ref[...] = mat_nt(block_ref[...], inv_ref[0:order, :])


def orth_kernel(block_ref, out_ref, rest_ref, inv_ref):
    factor_and_apply(block_ref, out_ref, rest_ref, inv_ref)


def power_orth_kernel(gram_ref, sub_ref, out_ref, rest_ref, inv_ref, block_ref):
    block_ref[...] = mat(gram_ref[...], sub_ref[...])
    factor_and_apply(block_ref, out_ref, rest_ref, inv_ref)


def orth_scratch(order):
    return [pltpu.VMEM((order, order), jnp.float32), pltpu.VMEM((order + PANEL, order), jnp.float32)]


def orthonormal(block):
    return pl.pallas_call(
        orth_kernel,
        out_shape=jax.ShapeDtypeStruct(block.shape, jnp.float32),
        scratch_shapes=orth_scratch(block.shape[1]),
    )(block)


def power_orthonormal(gram, subspace):
    return pl.pallas_call(
        power_orth_kernel,
        out_shape=jax.ShapeDtypeStruct(subspace.shape, jnp.float32),
        scratch_shapes=orth_scratch(subspace.shape[1]) + [pltpu.VMEM(subspace.shape, jnp.float32)],
    )(gram, subspace)


def scatter_sum(block, axis_name, parts):
    pieces = block.reshape(parts, block.shape[0] // parts, *block.shape[1:])
    return lax.all_to_all(pieces, axis_name, 0, 0, tiled=True).sum(0)


def gather_rows(block, axis_name, parts):
    copies = jnp.broadcast_to(block[None], (parts,) + block.shape)
    gathered = lax.all_to_all(copies, axis_name, 0, 0, tiled=True)
    return gathered.reshape(parts * block.shape[0], *block.shape[1:])


def sum_everywhere(block, sizes):
    partial = scatter_sum(block, "inner", sizes["inner"])
    partial = scatter_sum(partial, "outer", sizes["outer"])
    partial = gather_rows(partial, "outer", sizes["outer"])
    return gather_rows(partial, "inner", sizes["inner"])


def on_device(field_slab, start_block, sizes):
    gram_local = lax.dot_general(
        field_slab, field_slab, (((1, 2), (1, 2)), ((), ())),
        precision=lax.Precision.HIGHEST, preferred_element_type=jnp.float32,
    )
    subspace = orthonormal(start_block)
    gram_total = sum_everywhere(gram_local, sizes)
    for sweep_index in range(ITERS):
        subspace = power_orthonormal(gram_total, subspace)
    core_block = lax.dot_general(
        subspace, field_slab, (((0,), (0,)), ((), ())),
        precision=lax.Precision.HIGHEST, preferred_element_type=jnp.float32,
    )
    core_fibres = lax.all_to_all(core_block, "inner", split_axis=0, concat_axis=1, tiled=True)
    return (subspace, core_fibres)


def solution(mesh):
    sizes = dict(mesh.shape)
    in_specs = (P(None, "inner", "outer"), P())
    out_specs = (P(), P("inner", None, "outer"))
    return jax.shard_map(
        lambda f, s: on_device(f, s, sizes),
        mesh=mesh, in_specs=in_specs, out_specs=out_specs, check_vma=False,
    )
```

```python
import jax
import jax.numpy as jnp
from jax import lax
from jax.experimental import pallas as pl
from jax.experimental.pallas import tpu as pltpu
from jax.sharding import PartitionSpec as P

ITERS = 2

PANEL = 64
UNROLL = 1


def product(first_mat, second_mat):
    return jnp.dot(
        first_mat, second_mat, precision=lax.Precision.HIGHEST, preferred_element_type=jnp.float32
    )


def mat(first, second):
    return jnp.dot(first, second, precision=lax.Precision.HIGHEST, preferred_element_type=jnp.float32)


def mat_nt(first, second):
    return lax.dot_general(
        first, second, (((1,), (1,)), ((), ())),
        precision=lax.Precision.HIGHEST, preferred_element_type=jnp.float32,
    )


GROUP = 8


def leaf_inverse_factor(diag_block):
    size = diag_block.shape[0]
    wide = 2 * size
    sub = lax.broadcasted_iota(jnp.int32, (size, wide), 0)
    lane = lax.broadcasted_iota(jnp.int32, (size, wide), 1)
    sub_col = lax.broadcasted_iota(jnp.int32, (size, 1), 0)
    lane_row = lax.broadcasted_iota(jnp.int32, (1, wide), 1)
    joined = diag_block + jnp.where(lane == sub + size, 1.0, 0.0).astype(jnp.float32)

    def step(group, carry):
        rest, solved_rows = carry
        first = group * GROUP
        rows = [jnp.sum(jnp.where(sub == first + i, rest, 0.0), axis=0, keepdims=True) for i in range(GROUP)]
        cols = [jnp.sum(jnp.where(lane == first + i, rest, 0.0), axis=1, keepdims=True) for i in range(GROUP)]
        pivots = [
            [jnp.sum(jnp.where(lane_row == first + m, rows[i], 0.0), axis=1, keepdims=True) for m in range(i + 1)]
            for i in range(GROUP)
        ]
        low = [[None] * GROUP for _ in range(GROUP)]
        scales = []
        for i in range(GROUP):
            for r in range(i, GROUP):
                value = pivots[r][i]
                for m in range(i):
                    value = value - low[r][m] * low[i][m]
                if r == i:
                    scale = lax.rsqrt(value)
                    scales.append(scale)
                    low[i][i] = value * scale
                else:
                    low[r][i] = value * scales[i]
        factor_rows, factor_cols = [], []
        for i in range(GROUP):
            row, col = rows[i], cols[i]
            for m in range(i):
                row = row - low[i][m] * factor_rows[m]
                col = col - low[i][m] * factor_cols[m]
            factor_rows.append(jnp.where(lane_row >= first + i, row * scales[i], 0.0))
            factor_cols.append(jnp.where(sub_col >= first + i, col * scales[i], 0.0))
        for i in range(GROUP):
            rest = rest - factor_cols[i] * factor_rows[i]
            solved_rows = jnp.where(sub == first + i, factor_rows[i], solved_rows)
        return rest, solved_rows

    _, solved_rows = lax.fori_loop(0, size // GROUP, step, (joined, jnp.zeros_like(joined)), unroll=UNROLL)
    swapped = pltpu.roll(solved_rows, size, 1)
    return jnp.where(lane < size, swapped, 0.0)


def mat_tn(first, second):
    return lax.dot_general(
        first, second, (((0,), (0,)), ((), ())),
        precision=lax.Precision.HIGHEST, preferred_element_type=jnp.float32,
    )


def factor_and_apply(block_ref, out_ref, rest_ref, inv_ref):
    order = block_ref.shape[1]
    wide = 2 * PANEL
    block = block_ref[...]
    rest_ref[...] = mat_tn(block, block)
    eye_sub = lax.broadcasted_iota(jnp.int32, inv_ref.shape, 0)
    eye_lane = lax.broadcasted_iota(jnp.int32, inv_ref.shape, 1)
    inv_ref[...] = jnp.where(eye_sub == eye_lane, 1.0, 0.0).astype(jnp.float32)
    rows = lax.broadcasted_iota(jnp.int32, (order, 1), 0)
    lanes = lax.broadcasted_iota(jnp.int32, (order, wide), 1)
    panels = order // PANEL
    for panel in range(panels):
        low = panel * PANEL
        base = low - low % wide
        cols = rest_ref[:, base:base + wide]
        if low % wide:
            cols = pltpu.roll(cols, wide - low % wide, 1)
        cols = jnp.where(lanes < PANEL, cols, 0.0)
        diag_inv = leaf_inverse_factor(cols[low:low + PANEL, :])
        factor = jnp.where(rows >= low, mat_nt(cols, diag_inv), 0.0)
        solved = mat(diag_inv, inv_ref[low:low + wide, :])
        if panel + 1 < panels:
            rest_ref[...] = rest_ref[...] - mat_nt(factor, factor)
            below = jnp.where(rows >= low + PANEL, factor, 0.0)
            inv_ref[0:order, :] = inv_ref[0:order, :] - mat(below, solved)
        inv_ref[low:low + PANEL, :] = solved
    out_ref[...] = mat_nt(block_ref[...], inv_ref[0:order, :])


def orth_kernel(block_ref, out_ref, rest_ref, inv_ref):
    factor_and_apply(block_ref, out_ref, rest_ref, inv_ref)


def power_orth_kernel(gram_ref, sub_ref, out_ref, rest_ref, inv_ref, block_ref):
    block_ref[...] = mat(gram_ref[...], sub_ref[...])
    factor_and_apply(block_ref, out_ref, rest_ref, inv_ref)


def orth_scratch(order):
    return [pltpu.VMEM((order, order), jnp.float32), pltpu.VMEM((order + PANEL, order), jnp.float32)]


def orthonormal(block):
    return pl.pallas_call(
        orth_kernel,
        out_shape=jax.ShapeDtypeStruct(block.shape, jnp.float32),
        scratch_shapes=orth_scratch(block.shape[1]),
    )(block)


def power_orthonormal(gram, subspace):
    return pl.pallas_call(
        power_orth_kernel,
        out_shape=jax.ShapeDtypeStruct(subspace.shape, jnp.float32),
        scratch_shapes=orth_scratch(subspace.shape[1]) + [pltpu.VMEM(subspace.shape, jnp.float32)],
    )(gram, subspace)


def scatter_sum(block, axis_name, parts):
    pieces = block.reshape(parts, block.shape[0] // parts, *block.shape[1:])
    return lax.all_to_all(pieces, axis_name, 0, 0, tiled=True).sum(0)


def gather_rows(block, axis_name, parts):
    copies = jnp.broadcast_to(block[None], (parts,) + block.shape)
    gathered = lax.all_to_all(copies, axis_name, 0, 0, tiled=True)
    return gathered.reshape(parts * block.shape[0], *block.shape[1:])


def sum_everywhere(block, sizes):
    partial = scatter_sum(block, "inner", sizes["inner"])
    partial = scatter_sum(partial, "outer", sizes["outer"])
    partial = gather_rows(partial, "outer", sizes["outer"])
    return gather_rows(partial, "inner", sizes["inner"])


def on_device(field_slab, start_block, sizes):
    gram_local = lax.dot_general(
        field_slab, field_slab, (((1, 2), (1, 2)), ((), ())),
        precision=lax.Precision.HIGHEST, preferred_element_type=jnp.float32,
    )
    subspace = orthonormal(start_block)
    gram_total = sum_everywhere(gram_local, sizes)
    for sweep_index in range(ITERS):
        subspace = power_orthonormal(gram_total, subspace)
    ranks = subspace.shape[1]
    parts = sizes["inner"]
    core_block = lax.dot_general(
        subspace, field_slab, (((0,), (0,)), ((), ())),
        precision=lax.Precision.HIGHEST, preferred_element_type=jnp.float32,
    ).reshape(parts, ranks // parts, field_slab.shape[1] * field_slab.shape[2])
    arrived = lax.all_to_all(core_block, "inner", 0, 0, tiled=True)
    arrived = arrived.reshape(parts, ranks // parts, field_slab.shape[1], field_slab.shape[2])
    core_fibres = jnp.transpose(arrived, (1, 0, 2, 3)).reshape(
        ranks // parts, parts * field_slab.shape[1], field_slab.shape[2]
    )
    return (subspace, core_fibres)


def solution(mesh):
    sizes = dict(mesh.shape)
    in_specs = (P(None, "inner", "outer"), P())
    out_specs = (P(), P("inner", None, "outer"))
    return jax.shard_map(
        lambda f, s: on_device(f, s, sizes),
        mesh=mesh, in_specs=in_specs, out_specs=out_specs, check_vma=False,
    )
```

```python
import jax
import jax.numpy as jnp
from jax import lax
from jax.experimental import pallas as pl
from jax.experimental.pallas import tpu as pltpu
from jax.sharding import PartitionSpec as P

ITERS = 2

PANEL = 64
UNROLL = 1


def product(first_mat, second_mat):
    return jnp.dot(
        first_mat, second_mat, precision=lax.Precision.HIGHEST, preferred_element_type=jnp.float32
    )


def mat(first, second):
    return jnp.dot(first, second, precision=lax.Precision.HIGHEST, preferred_element_type=jnp.float32)


def mat_nt(first, second):
    return lax.dot_general(
        first, second, (((1,), (1,)), ((), ())),
        precision=lax.Precision.HIGHEST, preferred_element_type=jnp.float32,
    )


GROUP = 8


def leaf_inverse_factor(diag_block):
    size = diag_block.shape[0]
    wide = 2 * size
    sub = lax.broadcasted_iota(jnp.int32, (size, wide), 0)
    lane = lax.broadcasted_iota(jnp.int32, (size, wide), 1)
    sub_col = lax.broadcasted_iota(jnp.int32, (size, 1), 0)
    lane_row = lax.broadcasted_iota(jnp.int32, (1, wide), 1)
    joined = diag_block + jnp.where(lane == sub + size, 1.0, 0.0).astype(jnp.float32)

    def step(group, carry):
        rest, solved_rows = carry
        first = group * GROUP
        rows = [jnp.sum(jnp.where(sub == first + i, rest, 0.0), axis=0, keepdims=True) for i in range(GROUP)]
        cols = [jnp.sum(jnp.where(lane == first + i, rest, 0.0), axis=1, keepdims=True) for i in range(GROUP)]
        pivots = [
            [jnp.sum(jnp.where(lane_row == first + m, rows[i], 0.0), axis=1, keepdims=True) for m in range(i + 1)]
            for i in range(GROUP)
        ]
        low = [[None] * GROUP for _ in range(GROUP)]
        scales = []
        for i in range(GROUP):
            for r in range(i, GROUP):
                value = pivots[r][i]
                for m in range(i):
                    value = value - low[r][m] * low[i][m]
                if r == i:
                    scale = lax.rsqrt(value)
                    scales.append(scale)
                    low[i][i] = value * scale
                else:
                    low[r][i] = value * scales[i]
        factor_rows, factor_cols = [], []
        for i in range(GROUP):
            row, col = rows[i], cols[i]
            for m in range(i):
                row = row - low[i][m] * factor_rows[m]
                col = col - low[i][m] * factor_cols[m]
            factor_rows.append(jnp.where(lane_row >= first + i, row * scales[i], 0.0))
            factor_cols.append(jnp.where(sub_col >= first + i, col * scales[i], 0.0))
        for i in range(GROUP):
            rest = rest - factor_cols[i] * factor_rows[i]
            solved_rows = jnp.where(sub == first + i, factor_rows[i], solved_rows)
        return rest, solved_rows

    _, solved_rows = lax.fori_loop(0, size // GROUP, step, (joined, jnp.zeros_like(joined)), unroll=UNROLL)
    swapped = pltpu.roll(solved_rows, size, 1)
    return jnp.where(lane < size, swapped, 0.0)


def mat_tn(first, second):
    return lax.dot_general(
        first, second, (((0,), (0,)), ((), ())),
        precision=lax.Precision.HIGHEST, preferred_element_type=jnp.float32,
    )


def factor_and_apply(block_ref, out_ref, rest_ref, inv_ref):
    order = block_ref.shape[1]
    wide = 2 * PANEL
    block = block_ref[...]
    rest_ref[...] = mat_tn(block, block)
    eye_sub = lax.broadcasted_iota(jnp.int32, inv_ref.shape, 0)
    eye_lane = lax.broadcasted_iota(jnp.int32, inv_ref.shape, 1)
    inv_ref[...] = jnp.where(eye_sub == eye_lane, 1.0, 0.0).astype(jnp.float32)
    panels = order // PANEL
    for panel in range(panels):
        low = panel * PANEL
        ahead = low + PANEL
        base = low - low % wide
        cols = rest_ref[low:order, base:base + wide]
        if low % wide:
            cols = pltpu.roll(cols, wide - low % wide, 1)
        lanes = lax.broadcasted_iota(jnp.int32, cols.shape, 1)
        cols = jnp.where(lanes < PANEL, cols, 0.0)
        diag_inv = leaf_inverse_factor(cols[0:PANEL, :])
        factor = mat_nt(cols, diag_inv)
        solved = mat(diag_inv, inv_ref[low:low + wide, :])
        if panel + 1 < panels:
            tail = factor[PANEL:, :]
            full = factor
            if low:
                full = jnp.concatenate([jnp.zeros((low, PANEL), jnp.float32), factor], axis=0)
            rest_ref[ahead:order, :] = rest_ref[ahead:order, :] - mat_nt(tail, full)
            inv_ref[ahead:order, :] = inv_ref[ahead:order, :] - mat(tail, solved)
        inv_ref[low:low + PANEL, :] = solved
    out_ref[...] = mat_nt(block_ref[...], inv_ref[0:order, :])


def orth_kernel(block_ref, out_ref, rest_ref, inv_ref):
    factor_and_apply(block_ref, out_ref, rest_ref, inv_ref)


def power_orth_kernel(gram_ref, sub_ref, out_ref, rest_ref, inv_ref, block_ref):
    block_ref[...] = mat(gram_ref[...], sub_ref[...])
    factor_and_apply(block_ref, out_ref, rest_ref, inv_ref)


def orth_scratch(order):
    return [pltpu.VMEM((order, order), jnp.float32), pltpu.VMEM((order + PANEL, order), jnp.float32)]


def orthonormal(block):
    return pl.pallas_call(
        orth_kernel,
        out_shape=jax.ShapeDtypeStruct(block.shape, jnp.float32),
        scratch_shapes=orth_scratch(block.shape[1]),
    )(block)


def power_orthonormal(gram, subspace):
    return pl.pallas_call(
        power_orth_kernel,
        out_shape=jax.ShapeDtypeStruct(subspace.shape, jnp.float32),
        scratch_shapes=orth_scratch(subspace.shape[1]) + [pltpu.VMEM(subspace.shape, jnp.float32)],
    )(gram, subspace)


def scatter_sum(block, axis_name, parts):
    pieces = block.reshape(parts, block.shape[0] // parts, *block.shape[1:])
    return lax.all_to_all(pieces, axis_name, 0, 0, tiled=True).sum(0)


def gather_rows(block, axis_name, parts):
    copies = jnp.broadcast_to(block[None], (parts,) + block.shape)
    gathered = lax.all_to_all(copies, axis_name, 0, 0, tiled=True)
    return gathered.reshape(parts * block.shape[0], *block.shape[1:])


def sum_everywhere(block, sizes):
    partial = scatter_sum(block, "inner", sizes["inner"])
    partial = scatter_sum(partial, "outer", sizes["outer"])
    partial = gather_rows(partial, "outer", sizes["outer"])
    return gather_rows(partial, "inner", sizes["inner"])


def on_device(field_slab, start_block, sizes):
    gram_local = lax.dot_general(
        field_slab, field_slab, (((1, 2), (1, 2)), ((), ())),
        precision=lax.Precision.HIGHEST, preferred_element_type=jnp.float32,
    )
    subspace = orthonormal(start_block)
    gram_total = sum_everywhere(gram_local, sizes)
    for sweep_index in range(ITERS):
        subspace = power_orthonormal(gram_total, subspace)
    core_block = lax.dot_general(
        subspace, field_slab, (((0,), (0,)), ((), ())),
        precision=lax.Precision.HIGHEST, preferred_element_type=jnp.float32,
    )
    core_fibres = lax.all_to_all(core_block, "inner", split_axis=0, concat_axis=1, tiled=True)
    return (subspace, core_fibres)


def solution(mesh):
    sizes = dict(mesh.shape)
    in_specs = (P(None, "inner", "outer"), P())
    out_specs = (P(), P("inner", None, "outer"))
    return jax.shard_map(
        lambda f, s: on_device(f, s, sizes),
        mesh=mesh, in_specs=in_specs, out_specs=out_specs, check_vma=False,
    )
```

```python
import jax
import jax.numpy as jnp
from jax import lax
from jax.experimental import pallas as pl
from jax.experimental.pallas import tpu as pltpu
from jax.sharding import PartitionSpec as P

ITERS = 2

PANEL = 64
UNROLL = 1


def product(first_mat, second_mat):
    return jnp.dot(
        first_mat, second_mat, precision=lax.Precision.HIGHEST, preferred_element_type=jnp.float32
    )


def mat(first, second):
    return jnp.dot(first, second, precision=lax.Precision.HIGHEST, preferred_element_type=jnp.float32)


def mat_nt(first, second):
    return lax.dot_general(
        first, second, (((1,), (1,)), ((), ())),
        precision=lax.Precision.HIGHEST, preferred_element_type=jnp.float32,
    )


GROUP = 8


def leaf_inverse_factor(diag_block):
    size = diag_block.shape[0]
    wide = 2 * size
    sub = lax.broadcasted_iota(jnp.int32, (size, wide), 0)
    lane = lax.broadcasted_iota(jnp.int32, (size, wide), 1)
    sub_col = lax.broadcasted_iota(jnp.int32, (size, 1), 0)
    lane_row = lax.broadcasted_iota(jnp.int32, (1, wide), 1)
    joined = diag_block + jnp.where(lane == sub + size, 1.0, 0.0).astype(jnp.float32)

    def step(group, carry):
        rest, solved_rows = carry
        first = group * GROUP
        rows = [jnp.sum(jnp.where(sub == first + i, rest, 0.0), axis=0, keepdims=True) for i in range(GROUP)]
        cols = [jnp.sum(jnp.where(lane == first + i, rest, 0.0), axis=1, keepdims=True) for i in range(GROUP)]
        pivots = [
            [jnp.sum(jnp.where(lane_row == first + m, rows[i], 0.0), axis=1, keepdims=True) for m in range(i + 1)]
            for i in range(GROUP)
        ]
        low = [[None] * GROUP for _ in range(GROUP)]
        scales = []
        for i in range(GROUP):
            for r in range(i, GROUP):
                value = pivots[r][i]
                for m in range(i):
                    value = value - low[r][m] * low[i][m]
                if r == i:
                    scale = lax.rsqrt(value)
                    scales.append(scale)
                    low[i][i] = value * scale
                else:
                    low[r][i] = value * scales[i]
        factor_rows, factor_cols = [], []
        for i in range(GROUP):
            row, col = rows[i], cols[i]
            for m in range(i):
                row = row - low[i][m] * factor_rows[m]
                col = col - low[i][m] * factor_cols[m]
            factor_rows.append(jnp.where(lane_row >= first + i, row * scales[i], 0.0))
            factor_cols.append(jnp.where(sub_col >= first + i, col * scales[i], 0.0))
        for i in range(GROUP):
            rest = rest - factor_cols[i] * factor_rows[i]
            solved_rows = jnp.where(sub == first + i, factor_rows[i], solved_rows)
        return rest, solved_rows

    _, solved_rows = lax.fori_loop(0, size // GROUP, step, (joined, jnp.zeros_like(joined)), unroll=UNROLL)
    swapped = pltpu.roll(solved_rows, size, 1)
    return jnp.where(lane < size, swapped, 0.0)


def mat_tn(first, second):
    return lax.dot_general(
        first, second, (((0,), (0,)), ((), ())),
        precision=lax.Precision.HIGHEST, preferred_element_type=jnp.float32,
    )


def factor_and_apply(block_ref, out_ref, rest_ref, inv_ref):
    order = block_ref.shape[1]
    wide = 2 * PANEL
    block = block_ref[...]
    rest_ref[...] = mat_tn(block, block)
    eye_sub = lax.broadcasted_iota(jnp.int32, inv_ref.shape, 0)
    eye_lane = lax.broadcasted_iota(jnp.int32, inv_ref.shape, 1)
    inv_ref[...] = jnp.where(eye_sub == eye_lane, 1.0, 0.0).astype(jnp.float32)
    panels = order // PANEL
    for panel in range(panels):
        low = panel * PANEL
        ahead = low + PANEL
        base = low - low % wide
        cols = rest_ref[low:order, base:base + wide]
        if low % wide:
            cols = pltpu.roll(cols, wide - low % wide, 1)
        lanes = lax.broadcasted_iota(jnp.int32, cols.shape, 1)
        cols = jnp.where(lanes < PANEL, cols, 0.0)
        diag_inv = leaf_inverse_factor(cols[0:PANEL, :])
        factor = mat_nt(cols, diag_inv)
        span = -(-ahead // wide) * wide
        solved = mat(diag_inv, inv_ref[low:low + wide, 0:span])
        if panel + 1 < panels:
            tail = factor[PANEL:, :]
            full = factor
            if low:
                full = jnp.concatenate([jnp.zeros((low, PANEL), jnp.float32), factor], axis=0)
            rest_ref[ahead:order, base:order] = rest_ref[ahead:order, base:order] - mat_nt(tail, full[base:, :])
            inv_ref[ahead:order, 0:span] = inv_ref[ahead:order, 0:span] - mat(tail, solved)
        inv_ref[low:low + PANEL, 0:span] = solved
    out_ref[...] = mat_nt(block_ref[...], inv_ref[0:order, :])


def orth_kernel(block_ref, out_ref, rest_ref, inv_ref):
    factor_and_apply(block_ref, out_ref, rest_ref, inv_ref)


def power_orth_kernel(gram_ref, sub_ref, out_ref, rest_ref, inv_ref, block_ref):
    block_ref[...] = mat(gram_ref[...], sub_ref[...])
    factor_and_apply(block_ref, out_ref, rest_ref, inv_ref)


def orth_scratch(order):
    return [pltpu.VMEM((order, order), jnp.float32), pltpu.VMEM((order + PANEL, order), jnp.float32)]


def orthonormal(block):
    return pl.pallas_call(
        orth_kernel,
        out_shape=jax.ShapeDtypeStruct(block.shape, jnp.float32),
        scratch_shapes=orth_scratch(block.shape[1]),
    )(block)


def power_orthonormal(gram, subspace):
    return pl.pallas_call(
        power_orth_kernel,
        out_shape=jax.ShapeDtypeStruct(subspace.shape, jnp.float32),
        scratch_shapes=orth_scratch(subspace.shape[1]) + [pltpu.VMEM(subspace.shape, jnp.float32)],
    )(gram, subspace)


def scatter_sum(block, axis_name, parts):
    pieces = block.reshape(parts, block.shape[0] // parts, *block.shape[1:])
    return lax.all_to_all(pieces, axis_name, 0, 0, tiled=True).sum(0)


def gather_rows(block, axis_name, parts):
    copies = jnp.broadcast_to(block[None], (parts,) + block.shape)
    gathered = lax.all_to_all(copies, axis_name, 0, 0, tiled=True)
    return gathered.reshape(parts * block.shape[0], *block.shape[1:])


def sum_everywhere(block, sizes):
    partial = scatter_sum(block, "inner", sizes["inner"])
    partial = scatter_sum(partial, "outer", sizes["outer"])
    partial = gather_rows(partial, "outer", sizes["outer"])
    return gather_rows(partial, "inner", sizes["inner"])


def on_device(field_slab, start_block, sizes):
    gram_local = lax.dot_general(
        field_slab, field_slab, (((1, 2), (1, 2)), ((), ())),
        precision=lax.Precision.HIGHEST, preferred_element_type=jnp.float32,
    )
    subspace = orthonormal(start_block)
    gram_total = sum_everywhere(gram_local, sizes)
    for sweep_index in range(ITERS):
        subspace = power_orthonormal(gram_total, subspace)
    core_block = lax.dot_general(
        subspace, field_slab, (((0,), (0,)), ((), ())),
        precision=lax.Precision.HIGHEST, preferred_element_type=jnp.float32,
    )
    core_fibres = lax.all_to_all(core_block, "inner", split_axis=0, concat_axis=1, tiled=True)
    return (subspace, core_fibres)


def solution(mesh):
    sizes = dict(mesh.shape)
    in_specs = (P(None, "inner", "outer"), P())
    out_specs = (P(), P("inner", None, "outer"))
    return jax.shard_map(
        lambda f, s: on_device(f, s, sizes),
        mesh=mesh, in_specs=in_specs, out_specs=out_specs, check_vma=False,
    )
```

```python
import jax
import jax.numpy as jnp
from jax import lax
from jax.experimental import pallas as pl
from jax.experimental.pallas import tpu as pltpu
from jax.sharding import PartitionSpec as P

ITERS = 2

PANEL = 64
UNROLL = 1


def product(first_mat, second_mat):
    return jnp.dot(
        first_mat, second_mat, precision=lax.Precision.HIGHEST, preferred_element_type=jnp.float32
    )


def mat(first, second):
    return jnp.dot(first, second, precision=lax.Precision.HIGHEST, preferred_element_type=jnp.float32)


def mat_nt(first, second):
    return lax.dot_general(
        first, second, (((1,), (1,)), ((), ())),
        precision=lax.Precision.HIGHEST, preferred_element_type=jnp.float32,
    )


GROUP = 8


def leaf_inverse_factor(diag_block):
    size = diag_block.shape[0]
    wide = 2 * size
    sub = lax.broadcasted_iota(jnp.int32, (size, wide), 0)
    lane = lax.broadcasted_iota(jnp.int32, (size, wide), 1)
    sub_col = lax.broadcasted_iota(jnp.int32, (size, 1), 0)
    lane_row = lax.broadcasted_iota(jnp.int32, (1, wide), 1)
    joined = diag_block + jnp.where(lane == sub + size, 1.0, 0.0).astype(jnp.float32)

    def step(group, carry):
        rest, solved_rows = carry
        first = group * GROUP
        rows = [jnp.sum(jnp.where(sub == first + i, rest, 0.0), axis=0, keepdims=True) for i in range(GROUP)]
        cols = [jnp.sum(jnp.where(lane == first + i, rest, 0.0), axis=1, keepdims=True) for i in range(GROUP)]
        pivots = [
            [jnp.sum(jnp.where(lane_row == first + m, rows[i], 0.0), axis=1, keepdims=True) for m in range(i + 1)]
            for i in range(GROUP)
        ]
        low = [[None] * GROUP for _ in range(GROUP)]
        scales = []
        for i in range(GROUP):
            for r in range(i, GROUP):
                value = pivots[r][i]
                for m in range(i):
                    value = value - low[r][m] * low[i][m]
                if r == i:
                    scale = lax.rsqrt(value)
                    scales.append(scale)
                    low[i][i] = value * scale
                else:
                    low[r][i] = value * scales[i]
        factor_rows, factor_cols = [], []
        for i in range(GROUP):
            row, col = rows[i], cols[i]
            for m in range(i):
                row = row - low[i][m] * factor_rows[m]
                col = col - low[i][m] * factor_cols[m]
            factor_rows.append(jnp.where(lane_row >= first + i, row * scales[i], 0.0))
            factor_cols.append(jnp.where(sub_col >= first + i, col * scales[i], 0.0))
        for i in range(GROUP):
            rest = rest - factor_cols[i] * factor_rows[i]
            solved_rows = jnp.where(sub == first + i, factor_rows[i], solved_rows)
        return rest, solved_rows

    _, solved_rows = lax.fori_loop(0, size // GROUP, step, (joined, jnp.zeros_like(joined)), unroll=UNROLL)
    swapped = pltpu.roll(solved_rows, size, 1)
    return jnp.where(lane < size, swapped, 0.0)


def mat_tn(first, second):
    return lax.dot_general(
        first, second, (((0,), (0,)), ((), ())),
        precision=lax.Precision.HIGHEST, preferred_element_type=jnp.float32,
    )


def factor_and_apply(block_ref, out_ref, rest_ref, inv_ref):
    order = block_ref.shape[1]
    wide = 2 * PANEL
    block = block_ref[...]
    rest_ref[...] = mat_tn(block, block)
    eye_sub = lax.broadcasted_iota(jnp.int32, inv_ref.shape, 0)
    eye_lane = lax.broadcasted_iota(jnp.int32, inv_ref.shape, 1)
    inv_ref[...] = jnp.where(eye_sub == eye_lane, 1.0, 0.0).astype(jnp.float32)
    panels = order // PANEL
    for panel in range(panels):
        low = panel * PANEL
        ahead = low + PANEL
        base = low - low % wide
        cols = rest_ref[low:order, base:base + wide]
        if low % wide:
            cols = pltpu.roll(cols, wide - low % wide, 1)
        lanes = lax.broadcasted_iota(jnp.int32, cols.shape, 1)
        cols = jnp.where(lanes < PANEL, cols, 0.0)
        diag_inv = leaf_inverse_factor(cols[0:PANEL, :])
        factor = mat_nt(cols, diag_inv)
        if low:
            solved = mat(diag_inv, inv_ref[low:low + wide, :])
        else:
            solved = jnp.concatenate([diag_inv, jnp.zeros((PANEL, order - wide), jnp.float32)], axis=1)
        if panel + 1 < panels:
            tail = factor[PANEL:, :]
            full = factor
            if low:
                full = jnp.concatenate([jnp.zeros((low, PANEL), jnp.float32), factor], axis=0)
            rest_ref[ahead:order, :] = rest_ref[ahead:order, :] - mat_nt(tail, full)
            inv_ref[ahead:order, :] = inv_ref[ahead:order, :] - mat(tail, solved)
        inv_ref[low:low + PANEL, :] = solved
    out_ref[...] = mat_nt(block_ref[...], inv_ref[0:order, :])


def orth_kernel(block_ref, out_ref, rest_ref, inv_ref):
    factor_and_apply(block_ref, out_ref, rest_ref, inv_ref)


def power_orth_kernel(gram_ref, sub_ref, out_ref, rest_ref, inv_ref, block_ref):
    block_ref[...] = mat(gram_ref[...], sub_ref[...])
    factor_and_apply(block_ref, out_ref, rest_ref, inv_ref)


def orth_scratch(order):
    return [pltpu.VMEM((order, order), jnp.float32), pltpu.VMEM((order + PANEL, order), jnp.float32)]


def orthonormal(block):
    return pl.pallas_call(
        orth_kernel,
        out_shape=jax.ShapeDtypeStruct(block.shape, jnp.float32),
        scratch_shapes=orth_scratch(block.shape[1]),
    )(block)


def power_orthonormal(gram, subspace):
    return pl.pallas_call(
        power_orth_kernel,
        out_shape=jax.ShapeDtypeStruct(subspace.shape, jnp.float32),
        scratch_shapes=orth_scratch(subspace.shape[1]) + [pltpu.VMEM(subspace.shape, jnp.float32)],
    )(gram, subspace)


def scatter_sum(block, axis_name, parts):
    pieces = block.reshape(parts, block.shape[0] // parts, *block.shape[1:])
    return lax.all_to_all(pieces, axis_name, 0, 0, tiled=True).sum(0)


def gather_rows(block, axis_name, parts):
    copies = jnp.broadcast_to(block[None], (parts,) + block.shape)
    gathered = lax.all_to_all(copies, axis_name, 0, 0, tiled=True)
    return gathered.reshape(parts * block.shape[0], *block.shape[1:])


def sum_everywhere(block, sizes):
    partial = scatter_sum(block, "inner", sizes["inner"])
    partial = scatter_sum(partial, "outer", sizes["outer"])
    partial = gather_rows(partial, "outer", sizes["outer"])
    return gather_rows(partial, "inner", sizes["inner"])


def on_device(field_slab, start_block, sizes):
    gram_local = lax.dot_general(
        field_slab, field_slab, (((1, 2), (1, 2)), ((), ())),
        precision=lax.Precision.HIGHEST, preferred_element_type=jnp.float32,
    )
    subspace = orthonormal(start_block)
    gram_total = sum_everywhere(gram_local, sizes)
    for sweep_index in range(ITERS):
        subspace = power_orthonormal(gram_total, subspace)
    core_block = lax.dot_general(
        subspace, field_slab, (((0,), (0,)), ((), ())),
        precision=lax.Precision.HIGHEST, preferred_element_type=jnp.float32,
    )
    core_fibres = lax.all_to_all(core_block, "inner", split_axis=0, concat_axis=1, tiled=True)
    return (subspace, core_fibres)


def solution(mesh):
    sizes = dict(mesh.shape)
    in_specs = (P(None, "inner", "outer"), P())
    out_specs = (P(), P("inner", None, "outer"))
    return jax.shard_map(
        lambda f, s: on_device(f, s, sizes),
        mesh=mesh, in_specs=in_specs, out_specs=out_specs, check_vma=False,
    )
```
